1024 devices in a mesh: seq: 64 (over x, z_lo, core), clip: 16 (over y, z_hi).
Axes of the slice: x: 8, y: 8, z: 8 (z_hi: 2, z_lo: 4; z = z_hi * 4 + z_lo), core: 2. Of those that a mesh axis runs over, the one named last changes fastest.
Arguments:
- frames_in: bfloat16 [16, 64, 128, 768], P('clip', 'seq'), may hold values from -6 to 6
- norm_gains: float32 [2, 768], replicated, may hold values from 0.5 to 1.5
- space_proj: bfloat16 [768, 2304], replicated, may hold values from -0.21875 to 0.21875
- space_out: bfloat16 [768, 768], replicated, may hold values from -0.21875 to 0.21875
- time_proj: bfloat16 [768, 2304], replicated, may hold values from -0.21875 to 0.21875
- time_out: bfloat16 [768, 768], replicated, may hold values from -0.21875 to 0.21875
- qk_gains: float32 [4, 768], replicated, may hold values from 1 to 2.5
Outputs:
- block_out: bfloat16 [16, 64, 128, 768], P('clip', 'seq')
- clip_embed: float32 [16, 768], P('clip')
- similarity: float32 [16, 16], P('clip')
The draws below stay inside these ranges and needn't reach their ends.
All inputs are finite; a program needn't handle non-finite values.
Results may differ from the reference program's by a relative error of at most 0.02.
Values may be sent and summed in bfloat16 or wider, within the bound.
No kernel may reach another device: no remote copies, remote signals or barrier semaphores. Data moves between devices by JAX's collectives and lax.ppermute only.
A program may use at most 32 MiB of HBM per device.

```python
import math
import jax
import jax.numpy as jnp
from jax import lax

D = 768
HEADS = 12
PATCHES = 128
FRAMES = 64
CLIPS = 16


def level_of(rng, shape, shards, least, high):
    def one(axis_at, blocks):
        heights = jax.random.uniform(jax.random.fold_in(jax.random.fold_in(rng, 6), axis_at), (blocks,), jnp.float32, least / len(shards), high / len(shards))
        return jnp.repeat(jnp.exp(heights), shape[axis_at] // blocks).reshape((-1,) + (1,) * (len(shape) - axis_at - 1))

    factor_of = one(*shards[0])
    for cut in shards[1:]:
        factor_of = factor_of * one(*cut)
    return factor_of


def bell_draw(rng, shape, scale, reach, shards=(), kind=jnp.bfloat16):
    values = scale * jax.random.normal(rng, shape, jnp.float32)
    if shards:
        values = values * level_of(rng, shape, shards, -0.22, 0.18)
    return jnp.clip(values, -reach, reach).astype(kind)


def setup_inputs(seed: int = 0) -> dict:
    arg_keys = jax.random.split(jax.random.key(seed), 8)
    return {
        "frames_in": bell_draw(arg_keys[0], (CLIPS, FRAMES, PATCHES, D), 1.0, 6.0, ((0, 16), (1, 64))),
        "norm_gains": jnp.clip(1.0 + 0.1 * jax.random.normal(arg_keys[1], (2, D), jnp.float32), 0.5, 1.5),
        "space_proj": bell_draw(arg_keys[2], (D, 3 * D), D ** -0.5, 0.21875),
        "space_out": bell_draw(arg_keys[3], (D, D), D ** -0.5, 0.21875),
        "time_proj": bell_draw(arg_keys[4], (D, 3 * D), D ** -0.5, 0.21875),
        "time_out": bell_draw(arg_keys[5], (D, D), D ** -0.5, 0.21875),
        "qk_gains": jnp.clip(jax.random.uniform(arg_keys[6], (4, D), jnp.float32, 1.0, 2.5), 1.0, 2.5),
    }


def layer_norm(values, gains_row):
    widened = values.astype(jnp.float32)
    average = lax.optimization_barrier(jnp.mean(widened, axis=-1, keepdims=True))
    centred = widened - average
    spread = lax.optimization_barrier(jnp.mean(centred * centred, axis=-1, keepdims=True))
    return (centred * lax.rsqrt(spread + 1e-05) * gains_row).astype(jnp.bfloat16)

def head_norm(values, gains_row):
    inverse = lax.rsqrt(lax.optimization_barrier(jnp.mean(values * values, axis=-1, keepdims=True)) + 1e-06)
    return (values * inverse * gains_row.reshape(HEADS, -1)).astype(jnp.bfloat16)

def attention(normed, proj, out_weight, gain_query, gain_key):
    channels = normed.shape[-1]
    leading = normed.shape[:-1]
    head_size = channels // HEADS
    projected = jnp.dot(normed.reshape(-1, channels), proj, preferred_element_type=jnp.float32)
    projected = projected.astype(jnp.bfloat16).reshape(leading + (3 * channels,))
    queries = projected[..., :channels].astype(jnp.float32).reshape(leading + (HEADS, head_size))
    key_part = projected[..., channels:2 * channels].astype(jnp.float32).reshape(leading + (HEADS, head_size))
    value_part = projected[..., 2 * channels:].reshape(leading + (HEADS, head_size))
    query_n = head_norm(queries, gain_query)
    key_n = head_norm(key_part, gain_key)
    scores = jnp.einsum('...lhe,...mhe->...hlm', query_n.astype(jnp.float32), key_n.astype(jnp.float32))
    scores = scores * (1.0 / math.sqrt(head_size))
    raised = jnp.exp(scores)
    attn_weights = (raised / lax.optimization_barrier(jnp.sum(raised, axis=-1, keepdims=True))).astype(jnp.bfloat16)
    context = jnp.einsum('...hlm,...mhe->...lhe', attn_weights.astype(jnp.float32), value_part.astype(jnp.float32))
    context = context.astype(jnp.bfloat16).reshape(-1, channels)
    branch = jnp.dot(context, out_weight, preferred_element_type=jnp.float32)
    return branch.reshape(leading + (channels,))

def reference(frames_in, norm_gains, space_proj, space_out, time_proj, time_out, qk_gains):

    def per_clip(clip_tokens):
        spatial_in = layer_norm(clip_tokens, norm_gains[0])
        branch = attention(spatial_in, space_proj, space_out, qk_gains[0], qk_gains[1])
        middle = (clip_tokens.astype(jnp.float32) + branch).astype(jnp.bfloat16)
        temporal_in = jnp.transpose(layer_norm(middle, norm_gains[1]), (1, 0, 2))
        temporal = attention(temporal_in, time_proj, time_out, qk_gains[2], qk_gains[3]).astype(jnp.bfloat16)
        temporal = jnp.transpose(temporal, (1, 0, 2))
        block_out = (middle.astype(jnp.float32) + temporal.astype(jnp.float32)).astype(jnp.bfloat16)
        pooled = lax.optimization_barrier(jnp.sum(block_out.astype(jnp.float32), axis=(0, 1))) / (FRAMES * PATCHES)
        return (block_out, pooled)
    block_out, pooled = lax.map(per_clip, frames_in)
    clip_embed = pooled * lax.rsqrt(lax.optimization_barrier(jnp.mean(pooled * pooled, axis=-1, keepdims=True)) + 1e-06)
    similarity = jnp.dot(clip_embed, clip_embed.T, precision=lax.Precision.HIGHEST, preferred_element_type=jnp.float32) / D
    return (block_out, clip_embed, similarity)
```

```python
import math

import jax
import jax.numpy as jnp
from jax import lax
from jax.sharding import PartitionSpec as P

D = 768
HEADS = 12


def from_everyone(array, axis):
    copies = jnp.broadcast_to(array, (lax.axis_size(axis), *array.shape))
    return lax.all_to_all(copies, axis, split_axis=0, concat_axis=0, tiled=True)


def over_copies(array, axis):
    return from_everyone(array, axis).sum(axis=0)


def laid_out(pieces, dim):
    pieces = jnp.moveaxis(pieces, 0, dim)
    dims = pieces.shape
    return pieces.reshape(*dims[:dim], dims[dim] * dims[dim + 1], *dims[dim + 2 :])


def collect(array, axis, dim):
    return laid_out(from_everyone(array, axis), dim)


def layer_norm(values, gains_row):
    widened = values.astype(jnp.float32)
    average = jnp.mean(widened, axis=-1, keepdims=True)
    centred = widened - average
    spread = jnp.mean(centred * centred, axis=-1, keepdims=True)
    return (centred * lax.rsqrt(spread + 1e-05) * gains_row).astype(jnp.bfloat16)


def head_norm(values, gains_row):
    inverse = lax.rsqrt(jnp.mean(values * values, axis=-1, keepdims=True) + 1e-06)
    return (values * inverse * gains_row.reshape(HEADS, -1)).astype(jnp.bfloat16)


def project(normed, proj):
    channels = normed.shape[-1]
    leading = normed.shape[:-1]
    projected = jnp.dot(normed.reshape(-1, channels), proj, preferred_element_type=jnp.float32)
    return projected.astype(jnp.bfloat16).reshape(leading + (proj.shape[1],))


def attention(projected, out_weight, gain_query, gain_key):
    channels = out_weight.shape[0]
    leading = projected.shape[:-1]
    head_size = channels // HEADS
    queries = projected[..., :channels].astype(jnp.float32).reshape(leading + (HEADS, head_size))
    key_part = (
        projected[..., channels : 2 * channels]
        .astype(jnp.float32)
        .reshape(leading + (HEADS, head_size))
    )
    value_part = projected[..., 2 * channels :].reshape(leading + (HEADS, head_size))
    query_n = head_norm(queries, gain_query)
    key_n = head_norm(key_part, gain_key)
    scores = jnp.einsum("...lhe,...mhe->...hlm", query_n, key_n, preferred_element_type=jnp.float32)
    scores = scores * (1.0 / math.sqrt(head_size))
    raised = jnp.exp(scores)
    attn_weights = (raised / jnp.sum(raised, axis=-1, keepdims=True)).astype(jnp.bfloat16)
    context = jnp.einsum(
        "...hlm,...mhe->...lhe", attn_weights, value_part, preferred_element_type=jnp.float32
    )
    context = context.astype(jnp.bfloat16).reshape(-1, channels)
    branch = jnp.dot(context, out_weight, preferred_element_type=jnp.float32)
    return branch.reshape(leading + (channels,))


def on_device(frames_in, norm_gains, space_proj, space_out, time_proj, time_out, qk_gains):
    clips_here, frames_here, patch_count, channels = frames_in.shape
    groups = lax.axis_size("seq")
    per_group = patch_count // groups
    spatial_in = layer_norm(frames_in, norm_gains[0])
    branch = attention(project(spatial_in, space_proj), space_out, qk_gains[0], qk_gains[1])
    middle = (frames_in.astype(jnp.float32) + branch).astype(jnp.bfloat16)
    temporal_in = layer_norm(middle, norm_gains[1])
    outgoing = temporal_in.reshape(clips_here, groups, per_group, frames_here, channels)
    arrived = attention(
        project(
            lax.all_to_all(outgoing, "seq", split_axis=1, concat_axis=3, tiled=True), time_proj
        ),
        time_out,
        qk_gains[2],
        qk_gains[3],
    ).astype(jnp.bfloat16)
    returned = lax.all_to_all(arrived, "seq", split_axis=3, concat_axis=1, tiled=True)
    returned = returned.reshape(clips_here, frames_here, patch_count, channels)
    block_out = (middle.astype(jnp.float32) + returned.astype(jnp.float32)).astype(jnp.bfloat16)
    local_sum = jnp.sum(block_out.astype(jnp.float32), axis=(1, 2))
    pooled_total = lax.psum(local_sum, "seq")
    pooled = pooled_total / (frames_here * patch_count * groups)
    clip_embed = pooled * lax.rsqrt(jnp.mean(pooled * pooled, axis=-1, keepdims=True) + 1e-06)
    all_embeds = lax.all_gather(clip_embed, "clip", axis=0, tiled=True)
    similarity = (
        jnp.dot(
            clip_embed,
            all_embeds.T,
            precision=lax.Precision.HIGHEST,
            preferred_element_type=jnp.float32,
        )
        / D
    )
    return (block_out, clip_embed, similarity)


def solution(mesh):
    return jax.shard_map(
        on_device,
        mesh=mesh,
        in_specs=(P("clip", "seq", None, None), P(), P(), P(), P(), P(), P()),
        out_specs=(P("clip", "seq", None, None), P("clip", None), P("clip", None)),
        check_vma=False,
    )
```

```python
import math

import jax
import jax.numpy as jnp
from jax import lax
from jax.sharding import PartitionSpec as P

D = 768
HEADS = 12


def from_everyone(array, axis):
    copies = jnp.broadcast_to(array, (lax.axis_size(axis), *array.shape))
    return lax.all_to_all(copies, axis, split_axis=0, concat_axis=0, tiled=True)


def over_copies(array, axis):
    return from_everyone(array, axis).sum(axis=0)


def laid_out(pieces, dim):
    pieces = jnp.moveaxis(pieces, 0, dim)
    dims = pieces.shape
    return pieces.reshape(*dims[:dim], dims[dim] * dims[dim + 1], *dims[dim + 2 :])


def collect(array, axis, dim):
    return laid_out(from_everyone(array, axis), dim)


def layer_norm(values, gains_row):
    widened = values.astype(jnp.float32)
    average = jnp.mean(widened, axis=-1, keepdims=True)
    centred = widened - average
    spread = jnp.mean(centred * centred, axis=-1, keepdims=True)
    return (centred * lax.rsqrt(spread + 1e-05) * gains_row).astype(jnp.bfloat16)


def head_norm(values, gains_row):
    inverse = lax.rsqrt(jnp.mean(values * values, axis=-1, keepdims=True) + 1e-06)
    return (values * inverse * gains_row.reshape(HEADS, -1)).astype(jnp.bfloat16)


def project(normed, proj):
    channels = normed.shape[-1]
    leading = normed.shape[:-1]
    projected = jnp.dot(normed.reshape(-1, channels), proj, preferred_element_type=jnp.float32)
    return projected.astype(jnp.bfloat16).reshape(leading + (proj.shape[1],))


def attention(projected, out_weight, gain_query, gain_key):
    channels = out_weight.shape[0]
    leading = projected.shape[:-1]
    head_size = channels // HEADS
    queries = projected[..., :channels].astype(jnp.float32).reshape(leading + (HEADS, head_size))
    key_part = (
        projected[..., channels : 2 * channels]
        .astype(jnp.float32)
        .reshape(leading + (HEADS, head_size))
    )
    value_part = projected[..., 2 * channels :].reshape(leading + (HEADS, head_size))
    query_n = head_norm(queries, gain_query)
    key_n = head_norm(key_part, gain_key)
    scores = jnp.einsum("...lhe,...mhe->...hlm", query_n, key_n, preferred_element_type=jnp.float32)
    scores = scores * (1.0 / math.sqrt(head_size))
    raised = jnp.exp(scores)
    attn_weights = (raised / jnp.sum(raised, axis=-1, keepdims=True)).astype(jnp.bfloat16)
    context = jnp.einsum(
        "...hlm,...mhe->...lhe", attn_weights, value_part, preferred_element_type=jnp.float32
    )
    context = context.astype(jnp.bfloat16).reshape(-1, channels)
    branch = jnp.dot(context, out_weight, preferred_element_type=jnp.float32)
    return branch.reshape(leading + (channels,))


def on_device(frames_in, norm_gains, space_proj, space_out, time_proj, time_out, qk_gains):
    clips_here, frames_here, patch_count, channels = frames_in.shape
    groups = lax.axis_size("seq")
    per_group = patch_count // groups
    spatial_in = layer_norm(frames_in, norm_gains[0])
    branch = attention(project(spatial_in, space_proj), space_out, qk_gains[0], qk_gains[1])
    middle = (frames_in.astype(jnp.float32) + branch).astype(jnp.bfloat16)
    outgoing = middle.reshape(clips_here, groups, per_group, frames_here, channels)
    arrived = lax.all_to_all(outgoing, "seq", split_axis=1, concat_axis=3, tiled=True)
    temporal_in = layer_norm(arrived, norm_gains[1])
    branch_t = attention(
        project(temporal_in, time_proj), time_out, qk_gains[2], qk_gains[3]
    ).astype(jnp.bfloat16)
    block_t = (arrived.astype(jnp.float32) + branch_t.astype(jnp.float32)).astype(jnp.bfloat16)
    partial = jnp.sum(block_t.astype(jnp.float32), axis=(2, 3), keepdims=True)
    high = partial.astype(jnp.bfloat16)
    low = (partial - high.astype(jnp.float32)).astype(jnp.bfloat16)
    spread_shape = (clips_here, 1, 1, block_t.shape[3], channels)
    payload = jnp.concatenate(
        [block_t, jnp.broadcast_to(high, spread_shape), jnp.broadcast_to(low, spread_shape)], axis=2
    )
    returned = lax.all_to_all(payload, "seq", split_axis=3, concat_axis=1, tiled=True)
    block_out = returned[:, :, :per_group].reshape(clips_here, frames_here, patch_count, channels)
    sums = returned[:, :, per_group:].astype(jnp.float32)
    pooled_total = jnp.sum(sums, axis=(1, 2, 3))
    pooled = pooled_total / (frames_here * patch_count * groups)
    clip_embed = pooled * lax.rsqrt(jnp.mean(pooled * pooled, axis=-1, keepdims=True) + 1e-06)
    all_embeds = collect(clip_embed, "clip", 0)
    similarity = (
        jnp.dot(
            clip_embed,
            all_embeds.T,
            precision=lax.Precision.HIGHEST,
            preferred_element_type=jnp.float32,
        )
        / D
    )
    return (block_out, clip_embed, similarity)


def solution(mesh):
    return jax.shard_map(
        on_device,
        mesh=mesh,
        in_specs=(P("clip", "seq", None, None), P(), P(), P(), P(), P(), P()),
        out_specs=(P("clip", "seq", None, None), P("clip", None), P("clip", None)),
        check_vma=False,
    )
```

```python
import functools
import math

import jax
import jax.numpy as jnp
from jax import lax
from jax.experimental import pallas as pl
from jax.experimental.pallas import tpu as pltpu
from jax.sharding import PartitionSpec as P

D = 768
HEADS = 12


def from_everyone(array, axis):
    copies = jnp.broadcast_to(array, (lax.axis_size(axis), *array.shape))
    return lax.all_to_all(copies, axis, split_axis=0, concat_axis=0, tiled=True)


def over_copies(array, axis):
    return from_everyone(array, axis).sum(axis=0)


def laid_out(pieces, dim):
    pieces = jnp.moveaxis(pieces, 0, dim)
    dims = pieces.shape
    return pieces.reshape(*dims[:dim], dims[dim] * dims[dim + 1], *dims[dim + 2 :])


def collect(array, axis, dim):
    return laid_out(from_everyone(array, axis), dim)


def layer_norm(values, gains_row):
    widened = values.astype(jnp.float32)
    average = jnp.mean(widened, axis=-1, keepdims=True)
    centred = widened - average
    spread = jnp.mean(centred * centred, axis=-1, keepdims=True)
    return (centred * lax.rsqrt(spread + 1e-05) * gains_row).astype(jnp.bfloat16)


def head_norm(values, gains_row):
    inverse = lax.rsqrt(jnp.mean(values * values, axis=-1, keepdims=True) + 1e-06)
    return (values * inverse * gains_row.reshape(HEADS, -1)).astype(jnp.bfloat16)


def project(normed, proj):
    channels = normed.shape[-1]
    leading = normed.shape[:-1]
    projected = jnp.dot(normed.reshape(-1, channels), proj, preferred_element_type=jnp.float32)
    return projected.astype(jnp.bfloat16).reshape(leading + (proj.shape[1],))


def attention(projected, out_weight, gain_query, gain_key):
    channels = out_weight.shape[0]
    leading = projected.shape[:-1]
    head_size = channels // HEADS
    queries = projected[..., :channels].astype(jnp.float32).reshape(leading + (HEADS, head_size))
    key_part = (
        projected[..., channels : 2 * channels]
        .astype(jnp.float32)
        .reshape(leading + (HEADS, head_size))
    )
    value_part = projected[..., 2 * channels :].reshape(leading + (HEADS, head_size))
    query_n = head_norm(queries, gain_query)
    key_n = head_norm(key_part, gain_key)
    scores = jnp.einsum("...lhe,...mhe->...hlm", query_n, key_n, preferred_element_type=jnp.float32)
    scores = scores * (1.0 / math.sqrt(head_size))
    raised = jnp.exp(scores)
    attn_weights = (raised / jnp.sum(raised, axis=-1, keepdims=True)).astype(jnp.bfloat16)
    context = jnp.einsum(
        "...hlm,...mhe->...lhe", attn_weights, value_part, preferred_element_type=jnp.float32
    )
    context = context.astype(jnp.bfloat16).reshape(-1, channels)
    branch = jnp.dot(context, out_weight, preferred_element_type=jnp.float32)
    return branch.reshape(leading + (channels,))


def attention_kernel(groups, temporal, x_ref, ln_ref, w_ref, wo_ref, gq_ref, gk_ref, out_ref, qkv_ref, ctx_ref):
    rows, channels = x_ref.shape
    pairs = channels // 128
    span = rows // groups
    widened = x_ref[...].astype(jnp.float32)
    average = jnp.mean(widened, axis=-1, keepdims=True)
    centred = widened - average
    spread = jnp.mean(centred * centred, axis=-1, keepdims=True)
    normed = (centred * lax.rsqrt(spread + 1e-05) * ln_ref[...]).astype(jnp.bfloat16)
    qkv_ref[...] = jnp.dot(normed, w_ref[...], preferred_element_type=jnp.float32).astype(jnp.bfloat16)
    lane = lax.broadcasted_iota(jnp.int32, (1, 128), 1)
    first = lane < 64

    def pair_norm(values, gains):
        squares = values * values
        even = jnp.sum(jnp.where(first, squares, 0.0), axis=-1, keepdims=True) * (1.0 / 64)
        odd = jnp.sum(jnp.where(first, 0.0, squares), axis=-1, keepdims=True) * (1.0 / 64)
        inverse = jnp.where(first, lax.rsqrt(even + 1e-06), lax.rsqrt(odd + 1e-06))
        return (values * inverse * gains).astype(jnp.bfloat16)

    for p in range(pairs):
        cols = slice(p * 128, (p + 1) * 128)
        queries = qkv_ref[:, p * 128 : (p + 1) * 128].astype(jnp.float32)
        keys = qkv_ref[:, channels + p * 128 : channels + (p + 1) * 128].astype(jnp.float32)
        values = qkv_ref[:, 2 * channels + p * 128 : 2 * channels + (p + 1) * 128]
        query_n = pair_norm(queries, gq_ref[:, cols])
        key_n = pair_norm(keys, gk_ref[:, cols])
        zero = jnp.zeros_like(query_n)
        heads = (jnp.where(first, query_n, zero), jnp.where(first, zero, query_n))
        for g in range(groups):
            part = slice(g * span, (g + 1) * span)
            outs = []
            for query_h in heads:
                scores = lax.dot_general(
                    query_h[part], key_n[part], (((1,), (1,)), ((), ())),
                    preferred_element_type=jnp.float32,
                ) * 0.125
                raised = jnp.exp(scores)
                weights = (raised / jnp.sum(raised, axis=-1, keepdims=True)).astype(jnp.bfloat16)
                outs.append(jnp.dot(weights, values[part], preferred_element_type=jnp.float32))
            ctx_ref[part, cols] = jnp.where(first, outs[0], outs[1]).astype(jnp.bfloat16)
    branch = jnp.dot(ctx_ref[...], wo_ref[...], preferred_element_type=jnp.float32)
    if temporal:
        branch = branch.astype(jnp.bfloat16).astype(jnp.float32)
    result = (x_ref[...].astype(jnp.float32) + branch).astype(jnp.bfloat16)
    out_ref[:rows, :] = result
    if temporal:
        partial = jnp.sum(result.astype(jnp.float32), axis=0, keepdims=True)
        high = partial.astype(jnp.bfloat16)
        low = (partial - high.astype(jnp.float32)).astype(jnp.bfloat16)
        out_ref[rows : rows + span, :] = jnp.broadcast_to(high, (span, channels))
        out_ref[rows + span :, :] = jnp.broadcast_to(low, (span, channels))


def attention_block(tokens, ln_gain, proj, out_weight, gain_query, gain_key, groups, temporal):
    rows, channels = tokens.shape
    span = rows // groups
    out_rows = rows + 2 * span if temporal else rows
    flops = 2 * rows * channels * 3 * channels + 2 * rows * channels * channels + 8 * rows * span * channels
    return pl.pallas_call(
        functools.partial(attention_kernel, groups, temporal),
        out_shape=jax.ShapeDtypeStruct((out_rows, channels), jnp.bfloat16),
        scratch_shapes=[
            pltpu.VMEM((rows, 3 * channels), jnp.bfloat16),
            pltpu.VMEM((rows, channels), jnp.bfloat16),
        ],
        cost_estimate=pl.CostEstimate(
            flops=flops,
            transcendentals=2 * rows * span * HEADS,
            bytes_accessed=2 * (4 * channels * channels + 2 * rows * channels + 2 * span * channels),
        ),
    )(
        tokens,
        ln_gain.reshape(1, channels),
        proj,
        out_weight,
        gain_query.reshape(1, channels),
        gain_key.reshape(1, channels),
    )


def on_device(frames_in, norm_gains, space_proj, space_out, time_proj, time_out, qk_gains):
    clips_here, frames_here, patch_count, channels = frames_in.shape
    groups = lax.axis_size("seq")
    per_group = patch_count // groups
    tokens = frames_in.reshape(clips_here * frames_here * patch_count, channels)
    middle = attention_block(
        tokens, norm_gains[0], space_proj, space_out, qk_gains[0], qk_gains[1],
        clips_here * frames_here, False,
    )
    outgoing = middle.reshape(clips_here, groups, per_group, frames_here, channels)
    arrived = lax.all_to_all(outgoing, "seq", split_axis=1, concat_axis=3, tiled=True)
    arrived = arrived.reshape(-1, channels)
    payload = attention_block(
        arrived, norm_gains[1], time_proj, time_out, qk_gains[2], qk_gains[3],
        clips_here * per_group, True,
    )
    payload = payload.reshape(clips_here, 1, per_group + 2, -1, channels)
    returned = lax.all_to_all(payload, "seq", split_axis=3, concat_axis=1, tiled=True)
    block_out = returned[:, :, :per_group].reshape(clips_here, frames_here, patch_count, channels)
    sums = returned[:, :, per_group:].astype(jnp.float32)
    pooled_total = jnp.sum(sums, axis=(1, 2, 3))
    pooled = pooled_total / (frames_here * patch_count * groups)
    clip_embed = pooled * lax.rsqrt(jnp.mean(pooled * pooled, axis=-1, keepdims=True) + 1e-06)
    all_embeds = collect(clip_embed, "clip", 0)
    similarity = (
        jnp.dot(
            clip_embed,
            all_embeds.T,
            precision=lax.Precision.HIGHEST,
            preferred_element_type=jnp.float32,
        )
        / D
    )
    return (block_out, clip_embed, similarity)


def solution(mesh):
    return jax.shard_map(
        on_device,
        mesh=mesh,
        in_specs=(P("clip", "seq", None, None), P(), P(), P(), P(), P(), P()),
        out_specs=(P("clip", "seq", None, None), P("clip", None), P("clip", None)),
        check_vma=False,
    )
```

```python
import functools
import math

import jax
import jax.numpy as jnp
from jax import lax
from jax.experimental import pallas as pl
from jax.experimental.pallas import tpu as pltpu
from jax.sharding import PartitionSpec as P

D = 768
HEADS = 12


def from_everyone(array, axis):
    copies = jnp.broadcast_to(array, (lax.axis_size(axis), *array.shape))
    return lax.all_to_all(copies, axis, split_axis=0, concat_axis=0, tiled=True)


def over_copies(array, axis):
    return from_everyone(array, axis).sum(axis=0)


def laid_out(pieces, dim):
    pieces = jnp.moveaxis(pieces, 0, dim)
    dims = pieces.shape
    return pieces.reshape(*dims[:dim], dims[dim] * dims[dim + 1], *dims[dim + 2 :])


def collect(array, axis, dim):
    return laid_out(from_everyone(array, axis), dim)


def layer_norm(values, gains_row):
    widened = values.astype(jnp.float32)
    average = jnp.mean(widened, axis=-1, keepdims=True)
    centred = widened - average
    spread = jnp.mean(centred * centred, axis=-1, keepdims=True)
    return (centred * lax.rsqrt(spread + 1e-05) * gains_row).astype(jnp.bfloat16)


def head_norm(values, gains_row):
    inverse = lax.rsqrt(jnp.mean(values * values, axis=-1, keepdims=True) + 1e-06)
    return (values * inverse * gains_row.reshape(HEADS, -1)).astype(jnp.bfloat16)


def project(normed, proj):
    channels = normed.shape[-1]
    leading = normed.shape[:-1]
    projected = jnp.dot(normed.reshape(-1, channels), proj, preferred_element_type=jnp.float32)
    return projected.astype(jnp.bfloat16).reshape(leading + (proj.shape[1],))


def attention(projected, out_weight, gain_query, gain_key):
    channels = out_weight.shape[0]
    leading = projected.shape[:-1]
    head_size = channels // HEADS
    queries = projected[..., :channels].astype(jnp.float32).reshape(leading + (HEADS, head_size))
    key_part = (
        projected[..., channels : 2 * channels]
        .astype(jnp.float32)
        .reshape(leading + (HEADS, head_size))
    )
    value_part = projected[..., 2 * channels :].reshape(leading + (HEADS, head_size))
    query_n = head_norm(queries, gain_query)
    key_n = head_norm(key_part, gain_key)
    scores = jnp.einsum("...lhe,...mhe->...hlm", query_n, key_n, preferred_element_type=jnp.float32)
    scores = scores * (1.0 / math.sqrt(head_size))
    raised = jnp.exp(scores)
    attn_weights = (raised / jnp.sum(raised, axis=-1, keepdims=True)).astype(jnp.bfloat16)
    context = jnp.einsum(
        "...hlm,...mhe->...lhe", attn_weights, value_part, preferred_element_type=jnp.float32
    )
    context = context.astype(jnp.bfloat16).reshape(-1, channels)
    branch = jnp.dot(context, out_weight, preferred_element_type=jnp.float32)
    return branch.reshape(leading + (channels,))


def attention_kernel(groups, temporal, x_ref, ln_ref, w_ref, wo_ref, gq_ref, gk_ref, out_ref, qkv_ref, ctx_ref):
    rows, channels = x_ref.shape
    pairs = channels // 128
    span = rows // groups
    widened = x_ref[...].astype(jnp.float32)
    average = jnp.mean(widened, axis=-1, keepdims=True)
    centred = widened - average
    spread = jnp.mean(centred * centred, axis=-1, keepdims=True)
    normed = (centred * lax.rsqrt(spread + 1e-05) * ln_ref[...]).astype(jnp.bfloat16)
    qkv_ref[...] = jnp.dot(normed, w_ref[...], preferred_element_type=jnp.float32).astype(jnp.bfloat16)
    lane = lax.broadcasted_iota(jnp.int32, (1, 128), 1)
    first = lane < 64

    def pair_norm(values, gains):
        squares = values * values
        even = jnp.sum(jnp.where(first, squares, 0.0), axis=-1, keepdims=True) * (1.0 / 64)
        odd = jnp.sum(jnp.where(first, 0.0, squares), axis=-1, keepdims=True) * (1.0 / 64)
        inverse = jnp.where(first, lax.rsqrt(even + 1e-06), lax.rsqrt(odd + 1e-06))
        return (values * inverse * gains).astype(jnp.bfloat16)

    for p in range(pairs):
        cols = slice(p * 128, (p + 1) * 128)
        queries = qkv_ref[:, p * 128 : (p + 1) * 128].astype(jnp.float32)
        keys = qkv_ref[:, channels + p * 128 : channels + (p + 1) * 128].astype(jnp.float32)
        values = qkv_ref[:, 2 * channels + p * 128 : 2 * channels + (p + 1) * 128]
        query_n = pair_norm(queries, gq_ref[:, cols])
        key_n = pair_norm(keys, gk_ref[:, cols])
        zero = jnp.zeros_like(query_n)
        heads = (jnp.where(first, query_n, zero), jnp.where(first, zero, query_n))
        for g in range(groups):
            part = slice(g * span, (g + 1) * span)
            outs = []
            for query_h in heads:
                scores = lax.dot_general(
                    query_h[part], key_n[part], (((1,), (1,)), ((), ())),
                    preferred_element_type=jnp.float32,
                ) * 0.125
                raised = jnp.exp(scores)
                weights = (raised / jnp.sum(raised, axis=-1, keepdims=True)).astype(jnp.bfloat16)
                outs.append(jnp.dot(weights, values[part], preferred_element_type=jnp.float32))
            ctx_ref[part, cols] = jnp.where(first, outs[0], outs[1]).astype(jnp.bfloat16)
    branch = jnp.dot(ctx_ref[...], wo_ref[...], preferred_element_type=jnp.float32)
    if temporal:
        branch = branch.astype(jnp.bfloat16).astype(jnp.float32)
    result = (x_ref[...].astype(jnp.float32) + branch).astype(jnp.bfloat16)
    out_ref[:rows, :] = result
    if temporal:
        partial = jnp.sum(result.astype(jnp.float32), axis=0, keepdims=True)
        high = partial.astype(jnp.bfloat16)
        low = (partial - high.astype(jnp.float32)).astype(jnp.bfloat16)
        out_ref[rows : rows + span, :] = jnp.broadcast_to(high, (span, channels))
        out_ref[rows + span :, :] = jnp.broadcast_to(low, (span, channels))


def attention_block(tokens, ln_gain, proj, out_weight, gain_query, gain_key, groups, temporal):
    rows, channels = tokens.shape
    span = rows // groups
    out_rows = rows + 2 * span if temporal else rows
    flops = 2 * rows * channels * 3 * channels + 2 * rows * channels * channels + 8 * rows * span * channels
    return pl.pallas_call(
        functools.partial(attention_kernel, groups, temporal),
        out_shape=jax.ShapeDtypeStruct((out_rows, channels), jnp.bfloat16),
        scratch_shapes=[
            pltpu.VMEM((rows, 3 * channels), jnp.bfloat16),
            pltpu.VMEM((rows, channels), jnp.bfloat16),
        ],
        cost_estimate=pl.CostEstimate(
            flops=flops,
            transcendentals=2 * rows * span * HEADS,
            bytes_accessed=2 * (4 * channels * channels + 2 * rows * channels + 2 * span * channels),
        ),
    )(
        tokens,
        ln_gain.reshape(1, channels),
        proj,
        out_weight,
        gain_query.reshape(1, channels),
        gain_key.reshape(1, channels),
    )


def on_device(frames_in, norm_gains, space_proj, space_out, time_proj, time_out, qk_gains):
    clips_here, frames_here, patch_count, channels = frames_in.shape
    groups = lax.axis_size("seq")
    per_group = patch_count // groups
    tokens = frames_in.reshape(clips_here * frames_here * patch_count, channels)
    middle = attention_block(
        tokens, norm_gains[0], space_proj, space_out, qk_gains[0], qk_gains[1],
        clips_here * frames_here, False,
    )
    outgoing = middle.reshape(clips_here, groups, per_group, frames_here, channels)
    arrived = lax.all_to_all(outgoing, "seq", split_axis=1, concat_axis=3, tiled=True)
    arrived = arrived.reshape(-1, channels)
    payload = attention_block(
        arrived, norm_gains[1], time_proj, time_out, qk_gains[2], qk_gains[3],
        clips_here * per_group, True,
    )
    payload = payload.reshape(clips_here, 1, per_group + 2, -1, channels)
    returned = lax.all_to_all(payload, "seq", split_axis=3, concat_axis=1, tiled=True)
    block_out = returned[:, :, :per_group].reshape(clips_here, frames_here, patch_count, channels)
    sums = returned[:, :, per_group:].astype(jnp.float32)
    pooled_total = jnp.sum(sums, axis=(1, 2, 3))
    pooled = pooled_total / (frames_here * patch_count * groups)
    clip_embed = pooled * lax.rsqrt(jnp.mean(pooled * pooled, axis=-1, keepdims=True) + 1e-06)
    count = lax.axis_size("clip")
    pieces = [clip_embed] + [
        lax.ppermute(clip_embed, "clip", [(i, (i + shift) % count) for i in range(count)])
        for shift in range(1, count)
    ]
    pieces = jnp.concatenate(pieces, axis=0)
    here = lax.axis_index("clip")
    rows = lax.broadcasted_iota(jnp.int32, (count, count), 0)
    cols = lax.broadcasted_iota(jnp.int32, (count, count), 1)
    pick = (here - rows) % count == cols
    all_embeds = jnp.sum(jnp.where(pick[:, :, None], pieces[None, :, :], 0.0), axis=1)
    similarity = (
        jnp.dot(
            clip_embed,
            all_embeds.T,
            precision=lax.Precision.HIGHEST,
            preferred_element_type=jnp.float32,
        )
        / D
    )
    return (block_out, clip_embed, similarity)


def solution(mesh):
    return jax.shard_map(
        on_device,
        mesh=mesh,
        in_specs=(P("clip", "seq", None, None), P(), P(), P(), P(), P(), P()),
        out_specs=(P("clip", "seq", None, None), P("clip", None), P("clip", None)),
        check_vma=False,
    )
```

```python
import functools
import math

import jax
import jax.numpy as jnp
from jax import lax
from jax.experimental import pallas as pl
from jax.experimental.pallas import tpu as pltpu
from jax.sharding import PartitionSpec as P

D = 768
HEADS = 12


def from_everyone(array, axis):
    copies = jnp.broadcast_to(array, (lax.axis_size(axis), *array.shape))
    return lax.all_to_all(copies, axis, split_axis=0, concat_axis=0, tiled=True)


def over_copies(array, axis):
    return from_everyone(array, axis).sum(axis=0)


def laid_out(pieces, dim):
    pieces = jnp.moveaxis(pieces, 0, dim)
    dims = pieces.shape
    return pieces.reshape(*dims[:dim], dims[dim] * dims[dim + 1], *dims[dim + 2 :])


def collect(array, axis, dim):
    return laid_out(from_everyone(array, axis), dim)


def layer_norm(values, gains_row):
    widened = values.astype(jnp.float32)
    average = jnp.mean(widened, axis=-1, keepdims=True)
    centred = widened - average
    spread = jnp.mean(centred * centred, axis=-1, keepdims=True)
    return (centred * lax.rsqrt(spread + 1e-05) * gains_row).astype(jnp.bfloat16)


def head_norm(values, gains_row):
    inverse = lax.rsqrt(jnp.mean(values * values, axis=-1, keepdims=True) + 1e-06)
    return (values * inverse * gains_row.reshape(HEADS, -1)).astype(jnp.bfloat16)


def project(normed, proj):
    channels = normed.shape[-1]
    leading = normed.shape[:-1]
    projected = jnp.dot(normed.reshape(-1, channels), proj, preferred_element_type=jnp.float32)
    return projected.astype(jnp.bfloat16).reshape(leading + (proj.shape[1],))


def attention(projected, out_weight, gain_query, gain_key):
    channels = out_weight.shape[0]
    leading = projected.shape[:-1]
    head_size = channels // HEADS
    queries = projected[..., :channels].astype(jnp.float32).reshape(leading + (HEADS, head_size))
    key_part = (
        projected[..., channels : 2 * channels]
        .astype(jnp.float32)
        .reshape(leading + (HEADS, head_size))
    )
    value_part = projected[..., 2 * channels :].reshape(leading + (HEADS, head_size))
    query_n = head_norm(queries, gain_query)
    key_n = head_norm(key_part, gain_key)
    scores = jnp.einsum("...lhe,...mhe->...hlm", query_n, key_n, preferred_element_type=jnp.float32)
    scores = scores * (1.0 / math.sqrt(head_size))
    raised = jnp.exp(scores)
    attn_weights = (raised / jnp.sum(raised, axis=-1, keepdims=True)).astype(jnp.bfloat16)
    context = jnp.einsum(
        "...hlm,...mhe->...lhe", attn_weights, value_part, preferred_element_type=jnp.float32
    )
    context = context.astype(jnp.bfloat16).reshape(-1, channels)
    branch = jnp.dot(context, out_weight, preferred_element_type=jnp.float32)
    return branch.reshape(leading + (channels,))


def attention_kernel(groups, temporal, rows_of, x_ref, ln_ref, w_ref, wo_ref, qk_ref, out_ref, qkv_ref, ctx_ref):
    channels = w_ref.shape[0]
    ln_row, q_row, k_row = rows_of
    pieces = x_ref.shape[1] // channels
    tokens = jnp.concatenate(
        [x_ref[:, i * channels : (i + 1) * channels] for i in range(pieces)], axis=0
    )
    rows = tokens.shape[0]
    pairs = channels // 128
    span = rows // groups
    widened = tokens.astype(jnp.float32)
    average = jnp.mean(widened, axis=-1, keepdims=True)
    centred = widened - average
    spread = jnp.mean(centred * centred, axis=-1, keepdims=True)
    gain = ln_ref[ln_row : ln_row + 1, :]
    normed = (centred * lax.rsqrt(spread + 1e-05) * gain).astype(jnp.bfloat16)
    qkv_ref[...] = jnp.dot(normed, w_ref[...], preferred_element_type=jnp.float32).astype(jnp.bfloat16)
    lane = lax.broadcasted_iota(jnp.int32, (1, 128), 1)
    first = lane < 64

    def pair_norm(values, gains):
        squares = values * values
        even = jnp.sum(jnp.where(first, squares, 0.0), axis=-1, keepdims=True) * (1.0 / 64)
        odd = jnp.sum(jnp.where(first, 0.0, squares), axis=-1, keepdims=True) * (1.0 / 64)
        inverse = jnp.where(first, lax.rsqrt(even + 1e-06), lax.rsqrt(odd + 1e-06))
        return (values * inverse * gains).astype(jnp.bfloat16)

    for p in range(pairs):
        cols = slice(p * 128, (p + 1) * 128)
        queries = qkv_ref[:, p * 128 : (p + 1) * 128].astype(jnp.float32)
        keys = qkv_ref[:, channels + p * 128 : channels + (p + 1) * 128].astype(jnp.float32)
        values = qkv_ref[:, 2 * channels + p * 128 : 2 * channels + (p + 1) * 128]
        query_n = pair_norm(queries, qk_ref[q_row : q_row + 1, cols])
        key_n = pair_norm(keys, qk_ref[k_row : k_row + 1, cols])
        zero = jnp.zeros_like(query_n)
        heads = (jnp.where(first, query_n, zero), jnp.where(first, zero, query_n))
        for g in range(groups):
            part = slice(g * span, (g + 1) * span)
            outs = []
            for query_h in heads:
                scores = lax.dot_general(
                    query_h[part], key_n[part], (((1,), (1,)), ((), ())),
                    preferred_element_type=jnp.float32,
                ) * 0.125
                raised = jnp.exp(scores)
                weights = (raised / jnp.sum(raised, axis=-1, keepdims=True)).astype(jnp.bfloat16)
                outs.append(jnp.dot(weights, values[part], preferred_element_type=jnp.float32))
            ctx_ref[part, cols] = jnp.where(first, outs[0], outs[1]).astype(jnp.bfloat16)
    branch = jnp.dot(ctx_ref[...], wo_ref[...], preferred_element_type=jnp.float32)
    if temporal:
        branch = branch.astype(jnp.bfloat16).astype(jnp.float32)
    result = (widened + branch).astype(jnp.bfloat16)
    sends = out_ref.shape[0]
    blocks = rows // sends
    for i in range(blocks):
        out_ref[:, i * channels : (i + 1) * channels] = result[i * sends : (i + 1) * sends]
    if temporal:
        partial = jnp.sum(result.astype(jnp.float32), axis=0, keepdims=True)
        high = partial.astype(jnp.bfloat16)
        low = (partial - high.astype(jnp.float32)).astype(jnp.bfloat16)
        out_ref[:, blocks * channels : (blocks + 1) * channels] = jnp.broadcast_to(high, (sends, channels))
        out_ref[:, (blocks + 1) * channels :] = jnp.broadcast_to(low, (sends, channels))


def attention_block(tokens, norm_gains, proj, out_weight, qk_gains, rows_of, groups, temporal, sends):
    channels = proj.shape[0]
    rows = tokens.size // channels
    span = rows // groups
    lanes = (rows // sends + (2 if temporal else 0)) * channels
    flops = 2 * rows * channels * 3 * channels + 2 * rows * channels * channels + 8 * rows * span * channels
    return pl.pallas_call(
        functools.partial(attention_kernel, groups, temporal, rows_of),
        out_shape=jax.ShapeDtypeStruct((sends, lanes), jnp.bfloat16),
        scratch_shapes=[
            pltpu.VMEM((rows, 3 * channels), jnp.bfloat16),
            pltpu.VMEM((rows, channels), jnp.bfloat16),
        ],
        cost_estimate=pl.CostEstimate(
            flops=flops,
            transcendentals=2 * rows * span * HEADS,
            bytes_accessed=2 * (4 * channels * channels + 2 * rows * channels + sends * lanes),
        ),
    )(tokens, norm_gains, proj, out_weight, qk_gains)


def on_device(frames_in, norm_gains, space_proj, space_out, time_proj, time_out, qk_gains):
    clips_here, frames_here, patch_count, channels = frames_in.shape
    groups = lax.axis_size("seq")
    per_group = patch_count // groups
    tokens = frames_in.reshape(clips_here * frames_here * patch_count, channels)
    outgoing = attention_block(
        tokens, norm_gains, space_proj, space_out, qk_gains, (0, 0, 1),
        clips_here * frames_here, False, groups,
    )
    arrived = lax.all_to_all(outgoing, "seq", split_axis=0, concat_axis=0, tiled=True)
    payload = attention_block(
        arrived, norm_gains, time_proj, time_out, qk_gains, (1, 2, 3),
        clips_here * per_group, True, arrived.shape[0],
    )
    returned = lax.all_to_all(payload, "seq", split_axis=0, concat_axis=0, tiled=True)
    block_out = jnp.concatenate(
        [returned[:, i * channels : (i + 1) * channels] for i in range(per_group)], axis=0
    ).reshape(clips_here, frames_here, patch_count, channels)
    sums = returned[:, per_group * channels :].astype(jnp.float32).reshape(-1, 2, channels)
    pooled_total = jnp.sum(sums, axis=(0, 1)).reshape(clips_here, channels)
    pooled = pooled_total / (frames_here * patch_count * groups)
    clip_embed = pooled * lax.rsqrt(jnp.mean(pooled * pooled, axis=-1, keepdims=True) + 1e-06)
    all_embeds = collect(clip_embed, "clip", 0)
    similarity = (
        jnp.dot(
            clip_embed,
            all_embeds.T,
            precision=lax.Precision.HIGHEST,
            preferred_element_type=jnp.float32,
        )
        / D
    )
    return (block_out, clip_embed, similarity)


def solution(mesh):
    return jax.shard_map(
        on_device,
        mesh=mesh,
        in_specs=(P("clip", "seq", None, None), P(), P(), P(), P(), P(), P()),
        out_specs=(P("clip", "seq", None, None), P("clip", None), P("clip", None)),
        check_vma=False,
    )
```

```python
import functools
import math

import jax
import jax.numpy as jnp
from jax import lax
from jax.experimental import pallas as pl
from jax.experimental.pallas import tpu as pltpu
from jax.sharding import PartitionSpec as P

D = 768
HEADS = 12


def from_everyone(array, axis):
    copies = jnp.broadcast_to(array, (lax.axis_size(axis), *array.shape))
    return lax.all_to_all(copies, axis, split_axis=0, concat_axis=0, tiled=True)


def over_copies(array, axis):
    return from_everyone(array, axis).sum(axis=0)


def laid_out(pieces, dim):
    pieces = jnp.moveaxis(pieces, 0, dim)
    dims = pieces.shape
    return pieces.reshape(*dims[:dim], dims[dim] * dims[dim + 1], *dims[dim + 2 :])


def collect(array, axis, dim):
    return laid_out(from_everyone(array, axis), dim)


def layer_norm(values, gains_row):
    widened = values.astype(jnp.float32)
    average = jnp.mean(widened, axis=-1, keepdims=True)
    centred = widened - average
    spread = jnp.mean(centred * centred, axis=-1, keepdims=True)
    return (centred * lax.rsqrt(spread + 1e-05) * gains_row).astype(jnp.bfloat16)


def head_norm(values, gains_row):
    inverse = lax.rsqrt(jnp.mean(values * values, axis=-1, keepdims=True) + 1e-06)
    return (values * inverse * gains_row.reshape(HEADS, -1)).astype(jnp.bfloat16)


def project(normed, proj):
    channels = normed.shape[-1]
    leading = normed.shape[:-1]
    projected = jnp.dot(normed.reshape(-1, channels), proj, preferred_element_type=jnp.float32)
    return projected.astype(jnp.bfloat16).reshape(leading + (proj.shape[1],))


def attention(projected, out_weight, gain_query, gain_key):
    channels = out_weight.shape[0]
    leading = projected.shape[:-1]
    head_size = channels // HEADS
    queries = projected[..., :channels].astype(jnp.float32).reshape(leading + (HEADS, head_size))
    key_part = (
        projected[..., channels : 2 * channels]
        .astype(jnp.float32)
        .reshape(leading + (HEADS, head_size))
    )
    value_part = projected[..., 2 * channels :].reshape(leading + (HEADS, head_size))
    query_n = head_norm(queries, gain_query)
    key_n = head_norm(key_part, gain_key)
    scores = jnp.einsum("...lhe,...mhe->...hlm", query_n, key_n, preferred_element_type=jnp.float32)
    scores = scores * (1.0 / math.sqrt(head_size))
    raised = jnp.exp(scores)
    attn_weights = (raised / jnp.sum(raised, axis=-1, keepdims=True)).astype(jnp.bfloat16)
    context = jnp.einsum(
        "...hlm,...mhe->...lhe", attn_weights, value_part, preferred_element_type=jnp.float32
    )
    context = context.astype(jnp.bfloat16).reshape(-1, channels)
    branch = jnp.dot(context, out_weight, preferred_element_type=jnp.float32)
    return branch.reshape(leading + (channels,))


def attention_kernel(
    groups, temporal, x_ref, ln_ref, w_hbm, wo_hbm, gq_ref, gk_ref, out_ref, qkv_ref, ctx_ref,
    w_ref, wo_ref, sems,
):
    rows, channels = x_ref.shape
    loads = [
        pltpu.make_async_copy(
            w_hbm.at[:, j * channels : (j + 1) * channels],
            w_ref.at[:, j * channels : (j + 1) * channels],
            sems.at[j],
        )
        for j in range(3)
    ]
    loads.append(pltpu.make_async_copy(wo_hbm, wo_ref, sems.at[3]))
    for load in loads:
        load.start()
    pairs = channels // 128
    span = rows // groups
    widened = x_ref[...].astype(jnp.float32)
    average = jnp.mean(widened, axis=-1, keepdims=True)
    centred = widened - average
    spread = jnp.mean(centred * centred, axis=-1, keepdims=True)
    normed = (centred * lax.rsqrt(spread + 1e-05) * ln_ref[...]).astype(jnp.bfloat16)
    for j in range(3):
        loads[j].wait()
        block = slice(j * channels, (j + 1) * channels)
        qkv_ref[:, block] = jnp.dot(
            normed, w_ref[:, block], preferred_element_type=jnp.float32
        ).astype(jnp.bfloat16)
    lane = lax.broadcasted_iota(jnp.int32, (1, 128), 1)
    first = lane < 64

    def pair_norm(values, gains):
        squares = values * values
        even = jnp.sum(jnp.where(first, squares, 0.0), axis=-1, keepdims=True) * (1.0 / 64)
        odd = jnp.sum(jnp.where(first, 0.0, squares), axis=-1, keepdims=True) * (1.0 / 64)
        inverse = jnp.where(first, lax.rsqrt(even + 1e-06), lax.rsqrt(odd + 1e-06))
        return (values * inverse * gains).astype(jnp.bfloat16)

    for p in range(pairs):
        cols = slice(p * 128, (p + 1) * 128)
        queries = qkv_ref[:, p * 128 : (p + 1) * 128].astype(jnp.float32)
        keys = qkv_ref[:, channels + p * 128 : channels + (p + 1) * 128].astype(jnp.float32)
        values = qkv_ref[:, 2 * channels + p * 128 : 2 * channels + (p + 1) * 128]
        query_n = pair_norm(queries, gq_ref[:, cols])
        key_n = pair_norm(keys, gk_ref[:, cols])
        zero = jnp.zeros_like(query_n)
        heads = (jnp.where(first, query_n, zero), jnp.where(first, zero, query_n))
        for g in range(groups):
            part = slice(g * span, (g + 1) * span)
            outs = []
            for query_h in heads:
                scores = lax.dot_general(
                    query_h[part], key_n[part], (((1,), (1,)), ((), ())),
                    preferred_element_type=jnp.float32,
                ) * 0.125
                raised = jnp.exp(scores)
                weights = (raised / jnp.sum(raised, axis=-1, keepdims=True)).astype(jnp.bfloat16)
                outs.append(jnp.dot(weights, values[part], preferred_element_type=jnp.float32))
            ctx_ref[part, cols] = jnp.where(first, outs[0], outs[1]).astype(jnp.bfloat16)
    loads[3].wait()
    branch = jnp.dot(ctx_ref[...], wo_ref[...], preferred_element_type=jnp.float32)
    if temporal:
        branch = branch.astype(jnp.bfloat16).astype(jnp.float32)
    result = (x_ref[...].astype(jnp.float32) + branch).astype(jnp.bfloat16)
    out_ref[:rows, :] = result
    if temporal:
        partial = jnp.sum(result.astype(jnp.float32), axis=0, keepdims=True)
        high = partial.astype(jnp.bfloat16)
        low = (partial - high.astype(jnp.float32)).astype(jnp.bfloat16)
        out_ref[rows : rows + span, :] = jnp.broadcast_to(high, (span, channels))
        out_ref[rows + span :, :] = jnp.broadcast_to(low, (span, channels))


def attention_block(tokens, ln_gain, proj, out_weight, gain_query, gain_key, groups, temporal):
    rows, channels = tokens.shape
    span = rows // groups
    out_rows = rows + 2 * span if temporal else rows
    flops = 2 * rows * channels * 3 * channels + 2 * rows * channels * channels + 8 * rows * span * channels
    return pl.pallas_call(
        functools.partial(attention_kernel, groups, temporal),
        out_shape=jax.ShapeDtypeStruct((out_rows, channels), jnp.bfloat16),
        in_specs=[
            pl.BlockSpec(memory_space=pltpu.VMEM),
            pl.BlockSpec(memory_space=pltpu.VMEM),
            pl.BlockSpec(memory_space=pl.ANY),
            pl.BlockSpec(memory_space=pl.ANY),
            pl.BlockSpec(memory_space=pltpu.VMEM),
            pl.BlockSpec(memory_space=pltpu.VMEM),
        ],
        scratch_shapes=[
            pltpu.VMEM((rows, 3 * channels), jnp.bfloat16),
            pltpu.VMEM((rows, channels), jnp.bfloat16),
            pltpu.VMEM((channels, 3 * channels), jnp.bfloat16),
            pltpu.VMEM((channels, channels), jnp.bfloat16),
            pltpu.SemaphoreType.DMA((4,)),
        ],
        cost_estimate=pl.CostEstimate(
            flops=flops,
            transcendentals=2 * rows * span * HEADS,
            bytes_accessed=2 * (4 * channels * channels + 2 * rows * channels + 2 * span * channels),
        ),
    )(
        tokens,
        ln_gain.reshape(1, channels),
        proj,
        out_weight,
        gain_query.reshape(1, channels),
        gain_key.reshape(1, channels),
    )


def on_device(frames_in, norm_gains, space_proj, space_out, time_proj, time_out, qk_gains):
    clips_here, frames_here, patch_count, channels = frames_in.shape
    groups = lax.axis_size("seq")
    per_group = patch_count // groups
    tokens = frames_in.reshape(clips_here * frames_here * patch_count, channels)
    middle = attention_block(
        tokens, norm_gains[0], space_proj, space_out, qk_gains[0], qk_gains[1],
        clips_here * frames_here, False,
    )
    outgoing = middle.reshape(clips_here, groups, per_group, frames_here, channels)
    arrived = lax.all_to_all(outgoing, "seq", split_axis=1, concat_axis=3, tiled=True)
    arrived = arrived.reshape(-1, channels)
    payload = attention_block(
        arrived, norm_gains[1], time_proj, time_out, qk_gains[2], qk_gains[3],
        clips_here * per_group, True,
    )
    payload = payload.reshape(clips_here, 1, per_group + 2, -1, channels)
    returned = lax.all_to_all(payload, "seq", split_axis=3, concat_axis=1, tiled=True)
    block_out = returned[:, :, :per_group].reshape(clips_here, frames_here, patch_count, channels)
    sums = returned[:, :, per_group:].astype(jnp.float32)
    pooled_total = jnp.sum(sums, axis=(1, 2, 3))
    pooled = pooled_total / (frames_here * patch_count * groups)
    clip_embed = pooled * lax.rsqrt(jnp.mean(pooled * pooled, axis=-1, keepdims=True) + 1e-06)
    all_embeds = collect(clip_embed, "clip", 0)
    similarity = (
        jnp.dot(
            clip_embed,
            all_embeds.T,
            precision=lax.Precision.HIGHEST,
            preferred_element_type=jnp.float32,
        )
        / D
    )
    return (block_out, clip_embed, similarity)


def solution(mesh):
    return jax.shard_map(
        on_device,
        mesh=mesh,
        in_specs=(P("clip", "seq", None, None), P(), P(), P(), P(), P(), P()),
        out_specs=(P("clip", "seq", None, None), P("clip", None), P("clip", None)),
        check_vma=False,
    )
```

```python
import functools
import math

import jax
import jax.numpy as jnp
from jax import lax
from jax.experimental import pallas as pl
from jax.experimental.pallas import tpu as pltpu
from jax.sharding import PartitionSpec as P

D = 768
HEADS = 12


def from_everyone(array, axis):
    copies = jnp.broadcast_to(array, (lax.axis_size(axis), *array.shape))
    return lax.all_to_all(copies, axis, split_axis=0, concat_axis=0, tiled=True)


def over_copies(array, axis):
    return from_everyone(array, axis).sum(axis=0)


def laid_out(pieces, dim):
    pieces = jnp.moveaxis(pieces, 0, dim)
    dims = pieces.shape
    return pieces.reshape(*dims[:dim], dims[dim] * dims[dim + 1], *dims[dim + 2 :])


def collect(array, axis, dim):
    return laid_out(from_everyone(array, axis), dim)


def layer_norm(values, gains_row):
    widened = values.astype(jnp.float32)
    average = jnp.mean(widened, axis=-1, keepdims=True)
    centred = widened - average
    spread = jnp.mean(centred * centred, axis=-1, keepdims=True)
    return (centred * lax.rsqrt(spread + 1e-05) * gains_row).astype(jnp.bfloat16)


def head_norm(values, gains_row):
    inverse = lax.rsqrt(jnp.mean(values * values, axis=-1, keepdims=True) + 1e-06)
    return (values * inverse * gains_row.reshape(HEADS, -1)).astype(jnp.bfloat16)


def project(normed, proj):
    channels = normed.shape[-1]
    leading = normed.shape[:-1]
    projected = jnp.dot(normed.reshape(-1, channels), proj, preferred_element_type=jnp.float32)
    return projected.astype(jnp.bfloat16).reshape(leading + (proj.shape[1],))


def attention(projected, out_weight, gain_query, gain_key):
    channels = out_weight.shape[0]
    leading = projected.shape[:-1]
    head_size = channels // HEADS
    queries = projected[..., :channels].astype(jnp.float32).reshape(leading + (HEADS, head_size))
    key_part = (
        projected[..., channels : 2 * channels]
        .astype(jnp.float32)
        .reshape(leading + (HEADS, head_size))
    )
    value_part = projected[..., 2 * channels :].reshape(leading + (HEADS, head_size))
    query_n = head_norm(queries, gain_query)
    key_n = head_norm(key_part, gain_key)
    scores = jnp.einsum("...lhe,...mhe->...hlm", query_n, key_n, preferred_element_type=jnp.float32)
    scores = scores * (1.0 / math.sqrt(head_size))
    raised = jnp.exp(scores)
    attn_weights = (raised / jnp.sum(raised, axis=-1, keepdims=True)).astype(jnp.bfloat16)
    context = jnp.einsum(
        "...hlm,...mhe->...lhe", attn_weights, value_part, preferred_element_type=jnp.float32
    )
    context = context.astype(jnp.bfloat16).reshape(-1, channels)
    branch = jnp.dot(context, out_weight, preferred_element_type=jnp.float32)
    return branch.reshape(leading + (channels,))


def attention_kernel(groups, temporal, rows_of, x_ref, ln_ref, w_ref, wo_ref, qk_ref, out_ref, qkv_ref, ctx_ref):
    ln_row, q_row, k_row = rows_of
    rows, channels = x_ref.shape
    pairs = channels // 128
    span = rows // groups
    widened = x_ref[...].astype(jnp.float32)
    average = jnp.mean(widened, axis=-1, keepdims=True)
    centred = widened - average
    spread = jnp.mean(centred * centred, axis=-1, keepdims=True)
    gain = ln_ref[ln_row : ln_row + 1, :]
    normed = (centred * lax.rsqrt(spread + 1e-05) * gain).astype(jnp.bfloat16)
    qkv_ref[...] = jnp.dot(normed, w_ref[...], preferred_element_type=jnp.float32).astype(jnp.bfloat16)
    lane = lax.broadcasted_iota(jnp.int32, (1, 128), 1)
    first = lane < 64

    def pair_norm(values, gains):
        squares = values * values
        even = jnp.sum(jnp.where(first, squares, 0.0), axis=-1, keepdims=True) * (1.0 / 64)
        odd = jnp.sum(jnp.where(first, 0.0, squares), axis=-1, keepdims=True) * (1.0 / 64)
        inverse = jnp.where(first, lax.rsqrt(even + 1e-06), lax.rsqrt(odd + 1e-06))
        return (values * inverse * gains).astype(jnp.bfloat16)

    for p in range(pairs):
        cols = slice(p * 128, (p + 1) * 128)
        queries = qkv_ref[:, p * 128 : (p + 1) * 128].astype(jnp.float32)
        keys = qkv_ref[:, channels + p * 128 : channels + (p + 1) * 128].astype(jnp.float32)
        values = qkv_ref[:, 2 * channels + p * 128 : 2 * channels + (p + 1) * 128]
        query_n = pair_norm(queries, qk_ref[q_row : q_row + 1, cols])
        key_n = pair_norm(keys, qk_ref[k_row : k_row + 1, cols])
        zero = jnp.zeros_like(query_n)
        heads = (jnp.where(first, query_n, zero), jnp.where(first, zero, query_n))
        for g in range(groups):
            part = slice(g * span, (g + 1) * span)
            outs = []
            for query_h in heads:
                scores = lax.dot_general(
                    query_h[part], key_n[part], (((1,), (1,)), ((), ())),
                    preferred_element_type=jnp.float32,
                ) * 0.125
                raised = jnp.exp(scores)
                weights = (raised / jnp.sum(raised, axis=-1, keepdims=True)).astype(jnp.bfloat16)
                outs.append(jnp.dot(weights, values[part], preferred_element_type=jnp.float32))
            ctx_ref[part, cols] = jnp.where(first, outs[0], outs[1]).astype(jnp.bfloat16)
    branch = jnp.dot(ctx_ref[...], wo_ref[...], preferred_element_type=jnp.float32)
    if temporal:
        branch = branch.astype(jnp.bfloat16).astype(jnp.float32)
    result = (x_ref[...].astype(jnp.float32) + branch).astype(jnp.bfloat16)
    out_ref[:rows, :] = result
    if temporal:
        partial = jnp.sum(result.astype(jnp.float32), axis=0, keepdims=True)
        high = partial.astype(jnp.bfloat16)
        low = (partial - high.astype(jnp.float32)).astype(jnp.bfloat16)
        out_ref[rows : rows + span, :] = jnp.broadcast_to(high, (span, channels))
        out_ref[rows + span :, :] = jnp.broadcast_to(low, (span, channels))


def attention_block(tokens, norm_gains, proj, out_weight, qk_gains, rows_of, groups, temporal):
    rows, channels = tokens.shape
    span = rows // groups
    out_rows = rows + 2 * span if temporal else rows
    flops = 2 * rows * channels * 3 * channels + 2 * rows * channels * channels + 8 * rows * span * channels
    return pl.pallas_call(
        functools.partial(attention_kernel, groups, temporal, rows_of),
        out_shape=jax.ShapeDtypeStruct((out_rows, channels), jnp.bfloat16),
        scratch_shapes=[
            pltpu.VMEM((rows, 3 * channels), jnp.bfloat16),
            pltpu.VMEM((rows, channels), jnp.bfloat16),
        ],
        cost_estimate=pl.CostEstimate(
            flops=flops,
            transcendentals=2 * rows * span * HEADS,
            bytes_accessed=2 * (4 * channels * channels + 2 * rows * channels + 2 * span * channels),
        ),
    )(tokens, norm_gains, proj, out_weight, qk_gains)


def on_device(frames_in, norm_gains, space_proj, space_out, time_proj, time_out, qk_gains):
    clips_here, frames_here, patch_count, channels = frames_in.shape
    groups = lax.axis_size("seq")
    per_group = patch_count // groups
    tokens = frames_in.reshape(clips_here * frames_here * patch_count, channels)
    middle = attention_block(
        tokens, norm_gains, space_proj, space_out, qk_gains, (0, 0, 1),
        clips_here * frames_here, False,
    )
    outgoing = middle.reshape(clips_here, groups, per_group, frames_here, channels)
    arrived = lax.all_to_all(outgoing, "seq", split_axis=1, concat_axis=3, tiled=True)
    arrived = arrived.reshape(-1, channels)
    payload = attention_block(
        arrived, norm_gains, time_proj, time_out, qk_gains, (1, 2, 3),
        clips_here * per_group, True,
    )
    payload = payload.reshape(clips_here, 1, per_group + 2, -1, channels)
    returned = lax.all_to_all(payload, "seq", split_axis=3, concat_axis=1, tiled=True)
    block_out = returned[:, :, :per_group].reshape(clips_here, frames_here, patch_count, channels)
    sums = returned[:, :, per_group:].astype(jnp.float32)
    pooled_total = jnp.sum(sums, axis=(1, 2, 3))
    pooled = pooled_total / (frames_here * patch_count * groups)
    clip_embed = pooled * lax.rsqrt(jnp.mean(pooled * pooled, axis=-1, keepdims=True) + 1e-06)
    all_embeds = collect(clip_embed, "clip", 0)
    similarity = (
        jnp.dot(
            clip_embed,
            all_embeds.T,
            precision=lax.Precision.HIGHEST,
            preferred_element_type=jnp.float32,
        )
        / D
    )
    return (block_out, clip_embed, similarity)


def solution(mesh):
    return jax.shard_map(
        on_device,
        mesh=mesh,
        in_specs=(P("clip", "seq", None, None), P(), P(), P(), P(), P(), P()),
        out_specs=(P("clip", "seq", None, None), P("clip", None), P("clip", None)),
        check_vma=False,
    )
```

```python
import functools
import math

import jax
import jax.numpy as jnp
from jax import lax
from jax.experimental import pallas as pl
from jax.experimental.pallas import tpu as pltpu
from jax.sharding import PartitionSpec as P

D = 768
HEADS = 12


def from_everyone(array, axis):
    copies = jnp.broadcast_to(array, (lax.axis_size(axis), *array.shape))
    return lax.all_to_all(copies, axis, split_axis=0, concat_axis=0, tiled=True)


def over_copies(array, axis):
    return from_everyone(array, axis).sum(axis=0)


def laid_out(pieces, dim):
    pieces = jnp.moveaxis(pieces, 0, dim)
    dims = pieces.shape
    return pieces.reshape(*dims[:dim], dims[dim] * dims[dim + 1], *dims[dim + 2 :])


def collect(array, axis, dim):
    return laid_out(from_everyone(array, axis), dim)


def layer_norm(values, gains_row):
    widened = values.astype(jnp.float32)
    average = jnp.mean(widened, axis=-1, keepdims=True)
    centred = widened - average
    spread = jnp.mean(centred * centred, axis=-1, keepdims=True)
    return (centred * lax.rsqrt(spread + 1e-05) * gains_row).astype(jnp.bfloat16)


def head_norm(values, gains_row):
    inverse = lax.rsqrt(jnp.mean(values * values, axis=-1, keepdims=True) + 1e-06)
    return (values * inverse * gains_row.reshape(HEADS, -1)).astype(jnp.bfloat16)


def project(normed, proj):
    channels = normed.shape[-1]
    leading = normed.shape[:-1]
    projected = jnp.dot(normed.reshape(-1, channels), proj, preferred_element_type=jnp.float32)
    return projected.astype(jnp.bfloat16).reshape(leading + (proj.shape[1],))


def attention(projected, out_weight, gain_query, gain_key):
    channels = out_weight.shape[0]
    leading = projected.shape[:-1]
    head_size = channels // HEADS
    queries = projected[..., :channels].astype(jnp.float32).reshape(leading + (HEADS, head_size))
    key_part = (
        projected[..., channels : 2 * channels]
        .astype(jnp.float32)
        .reshape(leading + (HEADS, head_size))
    )
    value_part = projected[..., 2 * channels :].reshape(leading + (HEADS, head_size))
    query_n = head_norm(queries, gain_query)
    key_n = head_norm(key_part, gain_key)
    scores = jnp.einsum("...lhe,...mhe->...hlm", query_n, key_n, preferred_element_type=jnp.float32)
    scores = scores * (1.0 / math.sqrt(head_size))
    raised = jnp.exp(scores)
    attn_weights = (raised / jnp.sum(raised, axis=-1, keepdims=True)).astype(jnp.bfloat16)
    context = jnp.einsum(
        "...hlm,...mhe->...lhe", attn_weights, value_part, preferred_element_type=jnp.float32
    )
    context = context.astype(jnp.bfloat16).reshape(-1, channels)
    branch = jnp.dot(context, out_weight, preferred_element_type=jnp.float32)
    return branch.reshape(leading + (channels,))


def attention_kernel(groups, temporal, rows_of, x_ref, ln_ref, w_ref, wo_ref, qk_ref, out_ref, qkv_ref, ctx_ref):
    ln_row, q_row, k_row = rows_of
    rows, channels = x_ref.shape
    pairs = channels // 128
    span = rows // groups
    widened = x_ref[...].astype(jnp.float32)
    average = jnp.mean(widened, axis=-1, keepdims=True)
    centred = widened - average
    spread = jnp.mean(centred * centred, axis=-1, keepdims=True)
    gain = ln_ref[ln_row : ln_row + 1, :]
    normed = (centred * lax.rsqrt(spread + 1e-05) * gain).astype(jnp.bfloat16)
    qkv_ref[...] = jnp.dot(normed, w_ref[...], preferred_element_type=jnp.float32).astype(jnp.bfloat16)
    lane = lax.broadcasted_iota(jnp.int32, (1, 128), 1)
    same_group = (
        lax.broadcasted_iota(jnp.int32, (rows, rows), 0) // span
        == lax.broadcasted_iota(jnp.int32, (rows, rows), 1) // span
    )
    first = lane < 64

    def pair_norm(values, gains):
        squares = values * values
        even = jnp.sum(jnp.where(first, squares, 0.0), axis=-1, keepdims=True) * (1.0 / 64)
        odd = jnp.sum(jnp.where(first, 0.0, squares), axis=-1, keepdims=True) * (1.0 / 64)
        inverse = jnp.where(first, lax.rsqrt(even + 1e-06), lax.rsqrt(odd + 1e-06))
        return (values * inverse * gains).astype(jnp.bfloat16)

    for p in range(pairs):
        cols = slice(p * 128, (p + 1) * 128)
        queries = qkv_ref[:, p * 128 : (p + 1) * 128].astype(jnp.float32)
        keys = qkv_ref[:, channels + p * 128 : channels + (p + 1) * 128].astype(jnp.float32)
        values = qkv_ref[:, 2 * channels + p * 128 : 2 * channels + (p + 1) * 128]
        query_n = pair_norm(queries, qk_ref[q_row : q_row + 1, cols])
        key_n = pair_norm(keys, qk_ref[k_row : k_row + 1, cols])
        zero = jnp.zeros_like(query_n)
        heads = (jnp.where(first, query_n, zero), jnp.where(first, zero, query_n))
        outs = []
        for query_h in heads:
            scores = lax.dot_general(
                query_h, key_n, (((1,), (1,)), ((), ())),
                preferred_element_type=jnp.float32,
            ) * 0.125
            raised = jnp.exp(scores)
            if groups > 1:
                raised = jnp.where(same_group, raised, 0.0)
            weights = (raised / jnp.sum(raised, axis=-1, keepdims=True)).astype(jnp.bfloat16)
            outs.append(jnp.dot(weights, values, preferred_element_type=jnp.float32))
        ctx_ref[:, cols] = jnp.where(first, outs[0], outs[1]).astype(jnp.bfloat16)
    branch = jnp.dot(ctx_ref[...], wo_ref[...], preferred_element_type=jnp.float32)
    if temporal:
        branch = branch.astype(jnp.bfloat16).astype(jnp.float32)
    result = (x_ref[...].astype(jnp.float32) + branch).astype(jnp.bfloat16)
    out_ref[:rows, :] = result
    if temporal:
        partial = jnp.sum(result.astype(jnp.float32), axis=0, keepdims=True)
        high = partial.astype(jnp.bfloat16)
        low = (partial - high.astype(jnp.float32)).astype(jnp.bfloat16)
        out_ref[rows : rows + span, :] = jnp.broadcast_to(high, (span, channels))
        out_ref[rows + span :, :] = jnp.broadcast_to(low, (span, channels))


def attention_block(tokens, norm_gains, proj, out_weight, qk_gains, rows_of, groups, temporal):
    rows, channels = tokens.shape
    span = rows // groups
    out_rows = rows + 2 * span if temporal else rows
    flops = 2 * rows * channels * 3 * channels + 2 * rows * channels * channels + 8 * rows * span * channels
    return pl.pallas_call(
        functools.partial(attention_kernel, groups, temporal, rows_of),
        out_shape=jax.ShapeDtypeStruct((out_rows, channels), jnp.bfloat16),
        scratch_shapes=[
            pltpu.VMEM((rows, 3 * channels), jnp.bfloat16),
            pltpu.VMEM((rows, channels), jnp.bfloat16),
        ],
        cost_estimate=pl.CostEstimate(
            flops=flops,
            transcendentals=2 * rows * span * HEADS,
            bytes_accessed=2 * (4 * channels * channels + 2 * rows * channels + 2 * span * channels),
        ),
    )(tokens, norm_gains, proj, out_weight, qk_gains)


def on_device(frames_in, norm_gains, space_proj, space_out, time_proj, time_out, qk_gains):
    clips_here, frames_here, patch_count, channels = frames_in.shape
    groups = lax.axis_size("seq")
    per_group = patch_count // groups
    tokens = frames_in.reshape(clips_here * frames_here * patch_count, channels)
    middle = attention_block(
        tokens, norm_gains, space_proj, space_out, qk_gains, (0, 0, 1),
        clips_here * frames_here, False,
    )
    outgoing = middle.reshape(clips_here, groups, per_group, frames_here, channels)
    arrived = lax.all_to_all(outgoing, "seq", split_axis=1, concat_axis=3, tiled=True)
    arrived = arrived.reshape(-1, channels)
    payload = attention_block(
        arrived, norm_gains, time_proj, time_out, qk_gains, (1, 2, 3),
        clips_here * per_group, True,
    )
    payload = payload.reshape(clips_here, 1, per_group + 2, -1, channels)
    returned = lax.all_to_all(payload, "seq", split_axis=3, concat_axis=1, tiled=True)
    block_out = returned[:, :, :per_group].reshape(clips_here, frames_here, patch_count, channels)
    sums = returned[:, :, per_group:].astype(jnp.float32)
    pooled_total = jnp.sum(sums, axis=(1, 2, 3))
    pooled = pooled_total / (frames_here * patch_count * groups)
    clip_embed = pooled * lax.rsqrt(jnp.mean(pooled * pooled, axis=-1, keepdims=True) + 1e-06)
    all_embeds = collect(clip_embed, "clip", 0)
    similarity = (
        jnp.dot(
            clip_embed,
            all_embeds.T,
            precision=lax.Precision.HIGHEST,
            preferred_element_type=jnp.float32,
        )
        / D
    )
    return (block_out, clip_embed, similarity)


def solution(mesh):
    return jax.shard_map(
        on_device,
        mesh=mesh,
        in_specs=(P("clip", "seq", None, None), P(), P(), P(), P(), P(), P()),
        out_specs=(P("clip", "seq", None, None), P("clip", None), P("clip", None)),
        check_vma=False,
    )
```

```python
import functools
import math

import jax
import jax.numpy as jnp
from jax import lax
from jax.experimental import pallas as pl
from jax.experimental.pallas import tpu as pltpu
from jax.sharding import PartitionSpec as P

D = 768
HEADS = 12


def from_everyone(array, axis):
    copies = jnp.broadcast_to(array, (lax.axis_size(axis), *array.shape))
    return lax.all_to_all(copies, axis, split_axis=0, concat_axis=0, tiled=True)


def over_copies(array, axis):
    return from_everyone(array, axis).sum(axis=0)


def laid_out(pieces, dim):
    pieces = jnp.moveaxis(pieces, 0, dim)
    dims = pieces.shape
    return pieces.reshape(*dims[:dim], dims[dim] * dims[dim + 1], *dims[dim + 2 :])


def collect(array, axis, dim):
    return laid_out(from_everyone(array, axis), dim)


def layer_norm(values, gains_row):
    widened = values.astype(jnp.float32)
    average = jnp.mean(widened, axis=-1, keepdims=True)
    centred = widened - average
    spread = jnp.mean(centred * centred, axis=-1, keepdims=True)
    return (centred * lax.rsqrt(spread + 1e-05) * gains_row).astype(jnp.bfloat16)


def head_norm(values, gains_row):
    inverse = lax.rsqrt(jnp.mean(values * values, axis=-1, keepdims=True) + 1e-06)
    return (values * inverse * gains_row.reshape(HEADS, -1)).astype(jnp.bfloat16)


def project(normed, proj):
    channels = normed.shape[-1]
    leading = normed.shape[:-1]
    projected = jnp.dot(normed.reshape(-1, channels), proj, preferred_element_type=jnp.float32)
    return projected.astype(jnp.bfloat16).reshape(leading + (proj.shape[1],))


def attention(projected, out_weight, gain_query, gain_key):
    channels = out_weight.shape[0]
    leading = projected.shape[:-1]
    head_size = channels // HEADS
    queries = projected[..., :channels].astype(jnp.float32).reshape(leading + (HEADS, head_size))
    key_part = (
        projected[..., channels : 2 * channels]
        .astype(jnp.float32)
        .reshape(leading + (HEADS, head_size))
    )
    value_part = projected[..., 2 * channels :].reshape(leading + (HEADS, head_size))
    query_n = head_norm(queries, gain_query)
    key_n = head_norm(key_part, gain_key)
    scores = jnp.einsum("...lhe,...mhe->...hlm", query_n, key_n, preferred_element_type=jnp.float32)
    scores = scores * (1.0 / math.sqrt(head_size))
    raised = jnp.exp(scores)
    attn_weights = (raised / jnp.sum(raised, axis=-1, keepdims=True)).astype(jnp.bfloat16)
    context = jnp.einsum(
        "...hlm,...mhe->...lhe", attn_weights, value_part, preferred_element_type=jnp.float32
    )
    context = context.astype(jnp.bfloat16).reshape(-1, channels)
    branch = jnp.dot(context, out_weight, preferred_element_type=jnp.float32)
    return branch.reshape(leading + (channels,))


def attention_kernel(groups, temporal, rows_of, x_ref, ln_ref, w_ref, wo_ref, qk_ref, out_ref, qkv_ref, ctx_ref):
    ln_row, q_row, k_row = rows_of
    rows, channels = x_ref.shape
    pairs = channels // 128
    span = rows // groups
    widened = x_ref[...].astype(jnp.float32)
    average = jnp.mean(widened, axis=-1, keepdims=True)
    centred = widened - average
    spread = jnp.mean(centred * centred, axis=-1, keepdims=True)
    gain = ln_ref[ln_row : ln_row + 1, :]
    normed = (centred * lax.rsqrt(spread + 1e-05) * gain).astype(jnp.bfloat16)
    qkv_ref[...] = jnp.dot(normed, w_ref[...], preferred_element_type=jnp.float32).astype(jnp.bfloat16)
    lane = lax.broadcasted_iota(jnp.int32, (1, 128), 1)
    same_group = (
        lax.broadcasted_iota(jnp.int32, (rows, rows), 0) % groups
        == lax.broadcasted_iota(jnp.int32, (rows, rows), 1) % groups
    )
    first = lane < 64

    def pair_norm(values, gains):
        squares = values * values
        even = jnp.sum(jnp.where(first, squares, 0.0), axis=-1, keepdims=True) * (1.0 / 64)
        odd = jnp.sum(jnp.where(first, 0.0, squares), axis=-1, keepdims=True) * (1.0 / 64)
        inverse = jnp.where(first, lax.rsqrt(even + 1e-06), lax.rsqrt(odd + 1e-06))
        return (values * inverse * gains).astype(jnp.bfloat16)

    for p in range(pairs):
        cols = slice(p * 128, (p + 1) * 128)
        queries = qkv_ref[:, p * 128 : (p + 1) * 128].astype(jnp.float32)
        keys = qkv_ref[:, channels + p * 128 : channels + (p + 1) * 128].astype(jnp.float32)
        values = qkv_ref[:, 2 * channels + p * 128 : 2 * channels + (p + 1) * 128]
        query_n = pair_norm(queries, qk_ref[q_row : q_row + 1, cols])
        key_n = pair_norm(keys, qk_ref[k_row : k_row + 1, cols])
        zero = jnp.zeros_like(query_n)
        heads = (jnp.where(first, query_n, zero), jnp.where(first, zero, query_n))
        outs = []
        for query_h in heads:
            scores = lax.dot_general(
                query_h, key_n, (((1,), (1,)), ((), ())),
                preferred_element_type=jnp.float32,
            ) * 0.125
            raised = jnp.exp(scores)
            if groups > 1:
                raised = jnp.where(same_group, raised, 0.0)
            weights = (raised / jnp.sum(raised, axis=-1, keepdims=True)).astype(jnp.bfloat16)
            outs.append(jnp.dot(weights, values, preferred_element_type=jnp.float32))
        ctx_ref[:, cols] = jnp.where(first, outs[0], outs[1]).astype(jnp.bfloat16)
    branch = jnp.dot(ctx_ref[...], wo_ref[...], preferred_element_type=jnp.float32)
    if temporal:
        branch = branch.astype(jnp.bfloat16).astype(jnp.float32)
    result = (x_ref[...].astype(jnp.float32) + branch).astype(jnp.bfloat16)
    out_ref[:rows, :] = result
    if temporal:
        partial = jnp.sum(result.astype(jnp.float32), axis=0, keepdims=True)
        high = partial.astype(jnp.bfloat16)
        low = (partial - high.astype(jnp.float32)).astype(jnp.bfloat16)
        out_ref[rows : rows + span, :] = jnp.broadcast_to(high, (span, channels))
        out_ref[rows + span :, :] = jnp.broadcast_to(low, (span, channels))


def attention_block(tokens, norm_gains, proj, out_weight, qk_gains, rows_of, groups, temporal):
    rows, channels = tokens.shape
    span = rows // groups
    out_rows = rows + 2 * span if temporal else rows
    flops = 2 * rows * channels * 3 * channels + 2 * rows * channels * channels + 8 * rows * span * channels
    return pl.pallas_call(
        functools.partial(attention_kernel, groups, temporal, rows_of),
        out_shape=jax.ShapeDtypeStruct((out_rows, channels), jnp.bfloat16),
        scratch_shapes=[
            pltpu.VMEM((rows, 3 * channels), jnp.bfloat16),
            pltpu.VMEM((rows, channels), jnp.bfloat16),
        ],
        cost_estimate=pl.CostEstimate(
            flops=flops,
            transcendentals=2 * rows * span * HEADS,
            bytes_accessed=2 * (4 * channels * channels + 2 * rows * channels + 2 * span * channels),
        ),
    )(tokens, norm_gains, proj, out_weight, qk_gains)


def on_device(frames_in, norm_gains, space_proj, space_out, time_proj, time_out, qk_gains):
    clips_here, frames_here, patch_count, channels = frames_in.shape
    groups = lax.axis_size("seq")
    per_group = patch_count // groups
    tokens = frames_in.reshape(clips_here * frames_here * patch_count, channels)
    middle = attention_block(
        tokens, norm_gains, space_proj, space_out, qk_gains, (0, 0, 1),
        clips_here * frames_here, False,
    )
    outgoing = middle.reshape(clips_here, groups, per_group, frames_here, channels)
    arrived = lax.all_to_all(outgoing, "seq", split_axis=1, concat_axis=1, tiled=True)
    arrived = arrived.reshape(-1, channels)
    payload = attention_block(
        arrived, norm_gains, time_proj, time_out, qk_gains, (1, 2, 3),
        clips_here * per_group, True,
    )
    sends = payload.shape[0] // (per_group + 2)
    payload = jnp.concatenate(
        [
            payload[: per_group * sends].reshape(sends, per_group, channels),
            payload[per_group * sends :].reshape(2, sends, channels).transpose(1, 0, 2),
        ],
        axis=1,
    )
    returned = lax.all_to_all(payload, "seq", split_axis=0, concat_axis=0, tiled=True)
    block_out = returned[:, :per_group].reshape(clips_here, frames_here, patch_count, channels)
    sums = returned[:, per_group:].astype(jnp.float32)
    pooled_total = jnp.sum(sums, axis=(0, 1)).reshape(clips_here, channels)
    pooled = pooled_total / (frames_here * patch_count * groups)
    clip_embed = pooled * lax.rsqrt(jnp.mean(pooled * pooled, axis=-1, keepdims=True) + 1e-06)
    all_embeds = collect(clip_embed, "clip", 0)
    similarity = (
        jnp.dot(
            clip_embed,
            all_embeds.T,
            precision=lax.Precision.HIGHEST,
            preferred_element_type=jnp.float32,
        )
        / D
    )
    return (block_out, clip_embed, similarity)


def solution(mesh):
    return jax.shard_map(
        on_device,
        mesh=mesh,
        in_specs=(P("clip", "seq", None, None), P(), P(), P(), P(), P(), P()),
        out_specs=(P("clip", "seq", None, None), P("clip", None), P("clip", None)),
        check_vma=False,
    )
```

```python
import functools
import math

import jax
import jax.numpy as jnp
from jax import lax
from jax.experimental import pallas as pl
from jax.experimental.pallas import tpu as pltpu
from jax.sharding import PartitionSpec as P

D = 768
HEADS = 12


def from_everyone(array, axis):
    copies = jnp.broadcast_to(array, (lax.axis_size(axis), *array.shape))
    return lax.all_to_all(copies, axis, split_axis=0, concat_axis=0, tiled=True)


def over_copies(array, axis):
    return from_everyone(array, axis).sum(axis=0)


def laid_out(pieces, dim):
    pieces = jnp.moveaxis(pieces, 0, dim)
    dims = pieces.shape
    return pieces.reshape(*dims[:dim], dims[dim] * dims[dim + 1], *dims[dim + 2 :])


def collect(array, axis, dim):
    return laid_out(from_everyone(array, axis), dim)


def layer_norm(values, gains_row):
    widened = values.astype(jnp.float32)
    average = jnp.mean(widened, axis=-1, keepdims=True)
    centred = widened - average
    spread = jnp.mean(centred * centred, axis=-1, keepdims=True)
    return (centred * lax.rsqrt(spread + 1e-05) * gains_row).astype(jnp.bfloat16)


def head_norm(values, gains_row):
    inverse = lax.rsqrt(jnp.mean(values * values, axis=-1, keepdims=True) + 1e-06)
    return (values * inverse * gains_row.reshape(HEADS, -1)).astype(jnp.bfloat16)


def project(normed, proj):
    channels = normed.shape[-1]
    leading = normed.shape[:-1]
    projected = jnp.dot(normed.reshape(-1, channels), proj, preferred_element_type=jnp.float32)
    return projected.astype(jnp.bfloat16).reshape(leading + (proj.shape[1],))


def attention(projected, out_weight, gain_query, gain_key):
    channels = out_weight.shape[0]
    leading = projected.shape[:-1]
    head_size = channels // HEADS
    queries = projected[..., :channels].astype(jnp.float32).reshape(leading + (HEADS, head_size))
    key_part = (
        projected[..., channels : 2 * channels]
        .astype(jnp.float32)
        .reshape(leading + (HEADS, head_size))
    )
    value_part = projected[..., 2 * channels :].reshape(leading + (HEADS, head_size))
    query_n = head_norm(queries, gain_query)
    key_n = head_norm(key_part, gain_key)
    scores = jnp.einsum("...lhe,...mhe->...hlm", query_n, key_n, preferred_element_type=jnp.float32)
    scores = scores * (1.0 / math.sqrt(head_size))
    raised = jnp.exp(scores)
    attn_weights = (raised / jnp.sum(raised, axis=-1, keepdims=True)).astype(jnp.bfloat16)
    context = jnp.einsum(
        "...hlm,...mhe->...lhe", attn_weights, value_part, preferred_element_type=jnp.float32
    )
    context = context.astype(jnp.bfloat16).reshape(-1, channels)
    branch = jnp.dot(context, out_weight, preferred_element_type=jnp.float32)
    return branch.reshape(leading + (channels,))


def attention_kernel(groups, temporal, rows_of, x_ref, ln_ref, w_ref, wo_ref, qk_ref, out_ref, qkv_ref, ctx_ref):
    ln_row, q_row, k_row = rows_of
    rows, channels = x_ref.shape
    pairs = channels // 128
    span = rows // groups
    widened = x_ref[...].astype(jnp.float32)
    average = jnp.mean(widened, axis=-1, keepdims=True)
    centred = widened - average
    spread = jnp.mean(centred * centred, axis=-1, keepdims=True)
    gain = ln_ref[ln_row : ln_row + 1, :]
    normed = (centred * lax.rsqrt(spread + 1e-05) * gain).astype(jnp.bfloat16)
    qkv_ref[...] = jnp.dot(normed, w_ref[...], preferred_element_type=jnp.float32).astype(jnp.bfloat16)
    lane = lax.broadcasted_iota(jnp.int32, (1, 128), 1)
    same_group = (
        lax.broadcasted_iota(jnp.int32, (rows, rows), 0) // span
        == lax.broadcasted_iota(jnp.int32, (rows, rows), 1) // span
    )
    first = lane < 64

    def pair_norm(values, gains):
        squares = values * values
        even = jnp.sum(jnp.where(first, squares, 0.0), axis=-1, keepdims=True) * (1.0 / 64)
        odd = jnp.sum(jnp.where(first, 0.0, squares), axis=-1, keepdims=True) * (1.0 / 64)
        inverse = jnp.where(first, lax.rsqrt(even + 1e-06), lax.rsqrt(odd + 1e-06))
        return (values * inverse * gains).astype(jnp.bfloat16)

    for p in range(pairs):
        cols = slice(p * 128, (p + 1) * 128)
        queries = qkv_ref[:, p * 128 : (p + 1) * 128].astype(jnp.float32)
        keys = qkv_ref[:, channels + p * 128 : channels + (p + 1) * 128].astype(jnp.float32)
        values = qkv_ref[:, 2 * channels + p * 128 : 2 * channels + (p + 1) * 128]
        query_n = pair_norm(queries, qk_ref[q_row : q_row + 1, cols])
        key_n = pair_norm(keys, qk_ref[k_row : k_row + 1, cols])
        zero = jnp.zeros_like(query_n)
        heads = (jnp.where(first, query_n, zero), jnp.where(first, zero, query_n))
        outs = []
        for query_h in heads:
            scores = lax.dot_general(
                query_h, key_n, (((1,), (1,)), ((), ())),
                preferred_element_type=jnp.float32,
            ) * 0.125
            raised = jnp.exp(scores)
            if groups > 1:
                raised = jnp.where(same_group, raised, 0.0)
            weights = (raised / jnp.sum(raised, axis=-1, keepdims=True)).astype(jnp.bfloat16)
            outs.append(jnp.dot(weights, values, preferred_element_type=jnp.float32))
        ctx_ref[:, cols] = jnp.where(first, outs[0], outs[1]).astype(jnp.bfloat16)
    branch = jnp.dot(ctx_ref[...], wo_ref[...], preferred_element_type=jnp.float32)
    if temporal:
        branch = branch.astype(jnp.bfloat16).astype(jnp.float32)
    result = (x_ref[...].astype(jnp.float32) + branch).astype(jnp.bfloat16)
    out_ref[:rows, :] = result
    if temporal:
        partial = jnp.sum(result.astype(jnp.float32), axis=0, keepdims=True)
        high = partial.astype(jnp.bfloat16)
        low = (partial - high.astype(jnp.float32)).astype(jnp.bfloat16)
        out_ref[rows : rows + span, :] = jnp.broadcast_to(high, (span, channels))
        out_ref[rows + span :, :] = jnp.broadcast_to(low, (span, channels))


def attention_block(tokens, norm_gains, proj, out_weight, qk_gains, rows_of, groups, temporal):
    rows, channels = tokens.shape
    span = rows // groups
    out_rows = rows + 2 * span if temporal else rows
    flops = 2 * rows * channels * 3 * channels + 2 * rows * channels * channels + 8 * rows * span * channels
    return pl.pallas_call(
        functools.partial(attention_kernel, groups, temporal, rows_of),
        out_shape=jax.ShapeDtypeStruct((out_rows, channels), jnp.bfloat16),
        scratch_shapes=[
            pltpu.VMEM((rows, 3 * channels), jnp.bfloat16),
            pltpu.VMEM((rows, channels), jnp.bfloat16),
        ],
        cost_estimate=pl.CostEstimate(
            flops=flops,
            transcendentals=2 * rows * span * HEADS,
            bytes_accessed=2 * (4 * channels * channels + 2 * rows * channels + 2 * span * channels),
        ),
    )(tokens, norm_gains, proj, out_weight, qk_gains)


def on_device(frames_in, norm_gains, space_proj, space_out, time_proj, time_out, qk_gains):
    clips_here, frames_here, patch_count, channels = frames_in.shape
    groups = lax.axis_size("seq")
    per_group = patch_count // groups
    tokens = frames_in.reshape(clips_here * frames_here * patch_count, channels)
    middle = attention_block(
        tokens, norm_gains, space_proj, space_out, qk_gains, (0, 0, 1),
        clips_here * frames_here, False,
    )
    outgoing = middle.reshape(clips_here, groups, per_group, frames_here, channels)
    arrived = lax.all_to_all(outgoing, "seq", split_axis=1, concat_axis=3, tiled=True)
    arrived = arrived.reshape(-1, channels)
    payload = attention_block(
        arrived, norm_gains, time_proj, time_out, qk_gains, (1, 2, 3),
        clips_here * per_group, True,
    )
    payload = payload.reshape(clips_here, 1, per_group + 2, -1, channels)
    returned = lax.all_to_all(payload, "seq", split_axis=3, concat_axis=1, tiled=True)
    block_out = returned[:, :, :per_group].reshape(clips_here, frames_here, patch_count, channels)
    sums = returned[:, :, per_group:].astype(jnp.float32)
    pooled_total = jnp.sum(sums, axis=(1, 2, 3))
    pooled = pooled_total / (frames_here * patch_count * groups)
    all_pooled = collect(pooled, "clip", 0)
    clip_embed = pooled * lax.rsqrt(jnp.mean(pooled * pooled, axis=-1, keepdims=True) + 1e-06)
    all_embeds = all_pooled * lax.rsqrt(
        jnp.mean(all_pooled * all_pooled, axis=-1, keepdims=True) + 1e-06
    )
    similarity = (
        jnp.dot(
            clip_embed,
            all_embeds.T,
            precision=lax.Precision.HIGHEST,
            preferred_element_type=jnp.float32,
        )
        / D
    )
    return (block_out, clip_embed, similarity)


def solution(mesh):
    return jax.shard_map(
        on_device,
        mesh=mesh,
        in_specs=(P("clip", "seq", None, None), P(), P(), P(), P(), P(), P()),
        out_specs=(P("clip", "seq", None, None), P("clip", None), P("clip", None)),
        check_vma=False,
    )
```
